128 devices in a mesh: date: 16 (over z, x), space: 8 (over y, core).
Axes of the slice: x: 4, y: 4, z: 4, core: 2. Of those that a mesh axis runs over, the one named last changes fastest.
Arguments:
- frames: bfloat16 [64, 2048, 1024], P('date', 'space'), may hold values from -6 to 6
- cloud_mask: int32 [64, 2048], P('date', 'space'), may hold values from 0 to 1
- qkv_weight: bfloat16 [2, 1024, 3072], replicated, may hold values from -0.1875 to 0.1875
- out_weight: bfloat16 [2, 1024, 1024], replicated, may hold values from -0.1875 to 0.1875
- norm_gain: float32 [2, 1024], replicated, may hold values from 0.1 to 1.9
- head_norm_scale: float32 [2, 1024], replicated, may hold values from 0.1 to 1.9
- decay: float32 [2, 64, 16], P(None, 'date'), as said below
Outputs:
- forecast: bfloat16 [64, 2048, 1024], P('date', 'space')
The draws below stay inside these ranges and needn't reach their ends.
Inputs may be any that keep to these rules, and one draw needn't show every extreme that they name: `decay`: every entry lies strictly between 0 and 1.
All inputs are finite; a program needn't handle non-finite values.
Results may differ from the reference program's by a relative error of at most 0.0065.
Values may be sent and summed in bfloat16 or wider, within the bound.
No kernel may reach another device: no remote copies, remote signals or barrier semaphores. Data moves between devices by JAX's collectives and lax.ppermute only.
A program may use at most 128 MiB of HBM per device.

```python
import jax
import jax.numpy as jnp
from jax import lax

D = 1024
HEADS = 16
HEAD = 64
STACK_LEVELS = 2
DATE_DEV = 4
TIME_POINTS = 64
SPACE = 2048


def draw_decay(key, part):
    lookup_vectors = jax.random.split(key, 6)
    share = 0.5
    picker = jax.random.uniform(lookup_vectors[0], (STACK_LEVELS, 1, HEADS))
    slow = (picker < share) & (picker > jnp.min(picker, axis=2, keepdims=True))
    reach = jax.random.uniform(lookup_vectors[1], (STACK_LEVELS, 1, HEADS), minval=0.2, maxval=0.9)
    slow_rate = jnp.exp(-jnp.log(10.0) * reach / TIME_POINTS)
    fast_rate = jax.random.uniform(lookup_vectors[2], (STACK_LEVELS, 1, HEADS), minval=0.4, maxval=0.7)
    jitter = jax.random.uniform(lookup_vectors[3], (STACK_LEVELS, TIME_POINTS, HEADS), minval=0.97, maxval=1.0)
    recent_span = jax.random.uniform(lookup_vectors[4], (STACK_LEVELS, TIME_POINTS, 1)) < jnp.minimum(1.0, 3.0 / TIME_POINTS)
    level_index = jax.random.uniform(lookup_vectors[5], (STACK_LEVELS, TIME_POINTS, 1), minval=0.5, maxval=0.8)
    fading_rate = jnp.where(slow, slow_rate, fast_rate) * jitter
    fading_rate = jnp.where(recent_span, fading_rate * level_index, fading_rate)
    return fading_rate.astype(jnp.float32)


def draw_cloud_mask(key, part):
    streams = jax.random.split(jax.random.fold_in(key, 71), 3)
    tiles = jax.random.randint(streams[0], (TIME_POINTS, SPACE), 0, 4) < 3
    seasons = max(1, TIME_POINTS // 32)
    season_length = jax.random.randint(streams[1], (seasons,), 3 * DATE_DEV, 4 * DATE_DEV)
    season_start = jax.random.randint(streams[2], (seasons,), DATE_DEV, TIME_POINTS - 4 * DATE_DEV + 2)
    dates = jnp.arange(TIME_POINTS, dtype=jnp.int32)[:, None]
    inside = (dates >= season_start[None, :]) & (dates < season_start[None, :] + season_length[None, :])
    overcast = jnp.any(inside, axis=1)
    return jnp.where(overcast[:, None], 0, tiles.astype(jnp.int32)).astype(jnp.int32)


def block_scale(own_key, extent, shards, smallest, top_value):
    def one(position, blocks):
        heights = jax.random.uniform(jax.random.fold_in(jax.random.fold_in(own_key, 6), position), (blocks,), jnp.float32, smallest / len(shards), top_value / len(shards))
        return jnp.repeat(jnp.exp(heights), extent[position] // blocks).reshape((-1,) + (1,) * (len(extent) - position - 1))

    level = one(*shards[0])
    for cut in shards[1:]:
        level = level * one(*cut)
    return level


def normal_values(key, dims, scale, bound, pieces=(), kind=jnp.bfloat16):
    level = block_scale(key, dims, pieces, -0.22, 0.18) if pieces else 1.0
    array = jax.random.normal(key, dims, jnp.float32) * scale * level
    return jnp.minimum(jnp.maximum(array, -bound), bound).astype(kind)


def setup_inputs(seed: int = 0) -> dict:
    seeds = jax.random.split(jax.random.key(seed), 8)
    return {
        "frames": normal_values(seeds[0], (TIME_POINTS, SPACE, D), 1.0, 6.0, ((0, 16), (1, 8))),
        "cloud_mask": draw_cloud_mask(jax.random.fold_in(seeds[7], 71), 0),
        "qkv_weight": normal_values(seeds[2], (STACK_LEVELS, D, 3 * D), D ** -0.5, 0.1875),
        "out_weight": normal_values(seeds[3], (STACK_LEVELS, D, D), D ** -0.5, 0.1875),
        "norm_gain": jnp.clip(1.0 + 0.18 * jax.random.normal(seeds[4], (STACK_LEVELS, D), jnp.float32), 0.1, 1.9),
        "head_norm_scale": jnp.clip(1.0 + 0.18 * jax.random.normal(seeds[5], (STACK_LEVELS, D), jnp.float32), 0.1, 1.9),
        "decay": draw_decay(jax.random.fold_in(seeds[7], 71), 0),
    }


def feature(u):
    return jax.nn.elu(u) + 1.0

def one_layer(frames, cloud_mask, w_qkv, w_out, gain, h_gain, decay_l):

    def step(state, inputs):
        tokens, flags, persist_factor = inputs
        xf = tokens.astype(jnp.float32)
        in_msq = lax.optimization_barrier(jnp.mean(xf * xf, -1, keepdims=True)) + 1e-05
        normalized_output = (xf * lax.rsqrt(in_msq) * gain).astype(jnp.bfloat16)
        proj = jnp.dot(normalized_output, w_qkv, preferred_element_type=jnp.float32)
        flag_f = flags.astype(jnp.float32)[:, None]
        query = feature(proj[:, :D]).astype(jnp.bfloat16).reshape(-1, HEADS, HEAD)
        key = (feature(proj[:, D:2 * D]) * flag_f).astype(jnp.bfloat16).reshape(-1, HEADS, HEAD)
        value = proj[:, 2 * D:].astype(jnp.bfloat16).reshape(-1, HEADS, HEAD)
        kv = jnp.einsum('she,shf->hef', key.astype(jnp.float32), value.astype(jnp.float32))
        state = persist_factor[:, None, None] * state + kv
        state_b = state.astype(jnp.bfloat16)
        numer = jnp.einsum('she,hef->shf', query.astype(jnp.float32), state_b.astype(jnp.float32))
        head_msq = lax.optimization_barrier(jnp.mean(numer * numer, -1, keepdims=True)) + 1e-05
        numer = numer * lax.rsqrt(head_msq)
        mixed = (numer.reshape(-1, D) * h_gain).astype(jnp.bfloat16)
        result = (xf + jnp.dot(mixed, w_out, preferred_element_type=jnp.float32)).astype(jnp.bfloat16)
        return (state, result)
    start = jnp.zeros((HEADS, HEAD, HEAD), jnp.float32)
    _, result = lax.scan(step, start, (frames, cloud_mask, decay_l))
    return result

def reference(frames, cloud_mask, qkv_weight, out_weight, norm_gain, head_norm_scale, decay):
    current = frames
    for layer in range(STACK_LEVELS):
        current = one_layer(current, cloud_mask, qkv_weight[layer], out_weight[layer], norm_gain[layer], head_norm_scale[layer], decay[layer])
    return current
```

```python
import jax
import jax.numpy as jnp
from jax import lax
from jax.sharding import PartitionSpec as P

HEADS = 16
HEAD = 64
STACK_LEVELS = 2


def feature(u):
    return jax.nn.elu(u) + 1.0


def shards(frames, cloud_mask, qkv_weight, out_weight, norm_gain, head_norm_scale, decay):
    dates_here, tokens_here, width = frames.shape
    heads = HEADS
    n_space = lax.axis_size("space")
    n_date = lax.axis_size("date")
    me_space = lax.axis_index("space")
    me_date = lax.axis_index("date")
    mine = heads // n_space
    decay_all = lax.all_gather(decay, "date", axis=1, tiled=True)
    current = frames
    flag_f = cloud_mask.astype(jnp.float32)[:, :, None]
    for layer in range(STACK_LEVELS):
        xf = current.astype(jnp.float32)
        in_msq = jnp.mean(xf * xf, -1, keepdims=True) + 1e-05
        normalized_output = (xf * lax.rsqrt(in_msq) * norm_gain[layer]).astype(jnp.bfloat16)
        flat = normalized_output.reshape(-1, width)
        proj_kv = jnp.dot(flat, qkv_weight[layer, :, width:], preferred_element_type=jnp.float32)
        proj_kv = proj_kv.reshape(dates_here, tokens_here, 2 * width)
        key = (
            (feature(proj_kv[:, :, :width]) * flag_f)
            .astype(jnp.bfloat16)
            .reshape(dates_here, tokens_here, heads, HEAD)
        )
        value = proj_kv[:, :, width:].astype(jnp.bfloat16).reshape(dates_here, tokens_here, heads, HEAD)
        pairing_partial = jnp.einsum(
            "tshe,tshf->thef", key, value, preferred_element_type=jnp.float32
        )
        pieces = lax.all_to_all(pairing_partial, "space", 1, 1, tiled=True)
        kv = pieces.reshape(dates_here, n_space, mine, HEAD, HEAD).sum(1)

        dec = decay_all[layer].reshape(n_date, dates_here, heads)
        dec = lax.dynamic_slice_in_dim(dec, me_space * mine, mine, axis=2)
        local_dec = lax.dynamic_index_in_dim(dec, me_date, 0, keepdims=False)
        state = jnp.zeros((mine, HEAD, HEAD), jnp.float32)
        local_states = []
        for t in range(dates_here):
            state = local_dec[t][:, None, None] * state + kv[t]
            local_states.append(state)
        local_states = jnp.stack(local_states)
        kept = jnp.cumprod(local_dec, axis=0)
        totals = jnp.prod(dec, axis=1)

        gathered = lax.all_gather(state, "date", axis=0, tiled=False)
        pos = jnp.arange(n_date)
        between = (pos[None, :] > pos[:, None]) & (pos[None, :] < me_date)
        factors = jnp.where(between[:, :, None], totals[None, :, :], 1.0)
        weight = jnp.prod(factors, axis=1)
        weight = jnp.where((pos < me_date)[:, None], weight, 0.0)
        incoming = jnp.sum(weight[:, :, None, None] * gathered, axis=0)
        states = local_states + kept[:, :, None, None] * incoming[None]
        state_b = lax.all_gather(states.astype(jnp.bfloat16), "space", axis=1, tiled=True)

        proj_q = jnp.dot(flat, qkv_weight[layer, :, :width], preferred_element_type=jnp.float32)
        query = (
            feature(proj_q)
            .astype(jnp.bfloat16)
            .reshape(dates_here, tokens_here, heads, HEAD)
        )
        numer = jnp.einsum("tshe,thef->tshf", query, state_b, preferred_element_type=jnp.float32)
        head_msq = jnp.mean(numer * numer, -1, keepdims=True) + 1e-05
        numer = numer * lax.rsqrt(head_msq)
        mixed = (numer.reshape(dates_here, tokens_here, width) * head_norm_scale[layer]).astype(
            jnp.bfloat16
        )
        update = jnp.dot(
            mixed.reshape(-1, width), out_weight[layer], preferred_element_type=jnp.float32
        )
        current = (xf + update.reshape(dates_here, tokens_here, width)).astype(jnp.bfloat16)
    return current


def solution(mesh):
    placed = (
        P("date", "space", None),
        P("date", "space"),
        P(),
        P(),
        P(),
        P(),
        P(None, "date", None),
    )
    return jax.shard_map(
        shards, mesh=mesh, in_specs=placed, out_specs=P("date", "space", None), check_vma=False
    )
```

```python
import jax
import jax.numpy as jnp
from jax import lax
from jax.sharding import PartitionSpec as P

HEADS = 16
HEAD = 64
STACK_LEVELS = 2


def feature(u):
    return jax.nn.elu(u) + 1.0


def shards(frames, cloud_mask, qkv_weight, out_weight, norm_gain, head_norm_scale, decay):
    dates_here, tokens_here, width = frames.shape
    heads = HEADS
    n_space = lax.axis_size("space")
    n_date = lax.axis_size("date")
    me_space = lax.axis_index("space")
    me_date = lax.axis_index("date")
    mine = heads // n_space
    current = frames
    flag_f = cloud_mask.astype(jnp.float32)[:, :, None]
    for layer in range(STACK_LEVELS):
        xf = current.astype(jnp.float32)
        in_msq = jnp.mean(xf * xf, -1, keepdims=True) + 1e-05
        normalized_output = (xf * lax.rsqrt(in_msq) * norm_gain[layer]).astype(jnp.bfloat16)
        flat = normalized_output.reshape(-1, width)
        proj_kv = jnp.dot(flat, qkv_weight[layer, :, width:], preferred_element_type=jnp.float32)
        proj_kv = proj_kv.reshape(dates_here, tokens_here, 2 * width)
        key = (
            (feature(proj_kv[:, :, :width]) * flag_f)
            .astype(jnp.bfloat16)
            .reshape(dates_here, tokens_here, heads, HEAD)
        )
        value = proj_kv[:, :, width:].astype(jnp.bfloat16).reshape(dates_here, tokens_here, heads, HEAD)
        pairing_partial = jnp.einsum(
            "tshe,tshf->thef", key, value, preferred_element_type=jnp.float32
        )
        pieces = lax.all_to_all(pairing_partial, "space", 1, 1, tiled=True)
        kv = pieces.reshape(dates_here, n_space, mine, HEAD, HEAD).sum(1)

        local_dec = lax.dynamic_slice_in_dim(decay[layer], me_space * mine, mine, axis=1)
        state = jnp.zeros((mine, HEAD, HEAD), jnp.float32)
        local_states = []
        for t in range(dates_here):
            state = local_dec[t][:, None, None] * state + kv[t]
            local_states.append(state)
        local_states = jnp.stack(local_states)
        kept = jnp.cumprod(local_dec, axis=0)
        packed = jnp.concatenate(
            [state, jnp.broadcast_to(kept[-1][:, None, None], (mine, 8, HEAD))], axis=1
        )
        gathered = lax.all_gather(packed, "date", axis=0, tiled=False)
        totals = gathered[:, :, HEAD, 0]
        gathered = gathered[:, :, :HEAD, :]
        pos = jnp.arange(n_date)
        between = (pos[None, :] > pos[:, None]) & (pos[None, :] < me_date)
        factors = jnp.where(between[:, :, None], totals[None, :, :], 1.0)
        weight = jnp.prod(factors, axis=1)
        weight = jnp.where((pos < me_date)[:, None], weight, 0.0)
        incoming = jnp.sum(weight[:, :, None, None] * gathered, axis=0)
        states = local_states + kept[:, :, None, None] * incoming[None]
        state_b = lax.all_gather(states.astype(jnp.bfloat16), "space", axis=1, tiled=True)

        proj_q = jnp.dot(flat, qkv_weight[layer, :, :width], preferred_element_type=jnp.float32)
        query = (
            feature(proj_q)
            .astype(jnp.bfloat16)
            .reshape(dates_here, tokens_here, heads, HEAD)
        )
        numer = jnp.einsum("tshe,thef->tshf", query, state_b, preferred_element_type=jnp.float32)
        head_msq = jnp.mean(numer * numer, -1, keepdims=True) + 1e-05
        numer = numer * lax.rsqrt(head_msq)
        mixed = (numer.reshape(dates_here, tokens_here, width) * head_norm_scale[layer]).astype(
            jnp.bfloat16
        )
        update = jnp.dot(
            mixed.reshape(-1, width), out_weight[layer], preferred_element_type=jnp.float32
        )
        current = (xf + update.reshape(dates_here, tokens_here, width)).astype(jnp.bfloat16)
    return current


def solution(mesh):
    placed = (
        P("date", "space", None),
        P("date", "space"),
        P(),
        P(),
        P(),
        P(),
        P(None, "date", None),
    )
    return jax.shard_map(
        shards, mesh=mesh, in_specs=placed, out_specs=P("date", "space", None), check_vma=False
    )
```

```python
import jax
import jax.numpy as jnp
from jax import lax
from jax.sharding import PartitionSpec as P

HEADS = 16
HEAD = 64
STACK_LEVELS = 2


def feature(u):
    return jax.nn.elu(u) + 1.0


def shards(frames, cloud_mask, qkv_weight, out_weight, norm_gain, head_norm_scale, decay):
    dates_here, tokens_here, width = frames.shape
    heads = HEADS
    n_space = lax.axis_size("space")
    n_date = lax.axis_size("date")
    n_dev = n_date * n_space
    everyone = ("date", "space")
    me = lax.axis_index("date") * n_space + lax.axis_index("space")
    entries = heads * HEAD * HEAD // n_dev
    per_head = n_dev // heads
    dates_all = n_date * dates_here
    to_each = jnp.repeat(jnp.transpose(decay, (2, 0, 1)), per_head, axis=0)
    from_each = lax.all_to_all(to_each, everyone, 0, 0, tiled=True)
    my_decay = from_each.reshape(n_date, n_space, STACK_LEVELS, dates_here)[:, 0]
    my_decay = jnp.transpose(my_decay, (1, 0, 2)).reshape(STACK_LEVELS, dates_all)
    pos = jnp.arange(dates_all)
    current = frames
    flag_f = cloud_mask.astype(jnp.float32)[:, :, None]
    for layer in range(STACK_LEVELS):
        xf = current.astype(jnp.float32)
        in_msq = jnp.mean(xf * xf, -1, keepdims=True) + 1e-05
        normalized_output = (xf * lax.rsqrt(in_msq) * norm_gain[layer]).astype(jnp.bfloat16)
        flat = normalized_output.reshape(-1, width)
        proj_kv = jnp.dot(flat, qkv_weight[layer, :, width:], preferred_element_type=jnp.float32)
        proj_kv = proj_kv.reshape(dates_here, tokens_here, 2 * width)
        key = (
            (feature(proj_kv[:, :, :width]) * flag_f)
            .astype(jnp.bfloat16)
            .reshape(dates_here, tokens_here, heads, HEAD)
        )
        value = proj_kv[:, :, width:].astype(jnp.bfloat16).reshape(dates_here, tokens_here, heads, HEAD)
        pairing_partial = jnp.einsum(
            "tshe,tshf->thef", key, value, preferred_element_type=jnp.float32
        )
        pieces = lax.all_to_all(
            pairing_partial.reshape(dates_here, n_dev, entries), everyone, 1, 1, tiled=True
        )
        kv = pieces.reshape(dates_here, n_date, n_space, entries).sum(2)
        kv = jnp.transpose(kv, (1, 0, 2)).reshape(dates_all, entries)
        d = my_decay[layer]
        inside = (pos[None, None, :] > pos[None, :, None]) & (pos[None, None, :] <= pos[:, None, None])
        weight = jnp.prod(jnp.where(inside, d[None, None, :], 1.0), axis=2)
        weight = jnp.where(pos[None, :] <= pos[:, None], weight, 0.0)
        states = jnp.dot(weight, kv, precision=lax.Precision.HIGHEST, preferred_element_type=jnp.float32)
        state_b = states.astype(jnp.bfloat16).reshape(n_date, 1, dates_here, entries)
        outgoing = jnp.broadcast_to(state_b, (n_date, n_space, dates_here, entries)).reshape(
            n_dev, dates_here, entries
        )
        back = lax.all_to_all(outgoing, everyone, 0, 0, tiled=True)
        state_b = jnp.transpose(back, (1, 0, 2)).reshape(dates_here, heads, HEAD, HEAD)

        proj_q = jnp.dot(flat, qkv_weight[layer, :, :width], preferred_element_type=jnp.float32)
        query = (
            feature(proj_q)
            .astype(jnp.bfloat16)
            .reshape(dates_here, tokens_here, heads, HEAD)
        )
        numer = jnp.einsum("tshe,thef->tshf", query, state_b, preferred_element_type=jnp.float32)
        head_msq = jnp.mean(numer * numer, -1, keepdims=True) + 1e-05
        numer = numer * lax.rsqrt(head_msq)
        mixed = (numer.reshape(dates_here, tokens_here, width) * head_norm_scale[layer]).astype(
            jnp.bfloat16
        )
        update = jnp.dot(
            mixed.reshape(-1, width), out_weight[layer], preferred_element_type=jnp.float32
        )
        current = (xf + update.reshape(dates_here, tokens_here, width)).astype(jnp.bfloat16)
    return current


def solution(mesh):
    placed = (
        P("date", "space", None),
        P("date", "space"),
        P(),
        P(),
        P(),
        P(),
        P(None, "date", None),
    )
    return jax.shard_map(
        shards, mesh=mesh, in_specs=placed, out_specs=P("date", "space", None), check_vma=False
    )
```

```python
import jax
import jax.numpy as jnp
from jax import lax
from jax.experimental import pallas as pl
from jax.experimental.pallas import tpu as pltpu
from jax.sharding import PartitionSpec as P

HEADS = 16
HEAD = 64
STACK_LEVELS = 2


def feature(u):
    return jax.nn.elu(u) + 1.0


def kv_chunks(key, value, n_dev):
    dates, tokens, width = key.shape
    per_head = n_dev // HEADS
    rows = HEAD // per_head

    def body(k_ref, v_ref, o_ref):
        for t in range(dates):
            for h in range(HEADS):
                k = k_ref[t, :, h * HEAD : (h + 1) * HEAD]
                v = v_ref[t, :, h * HEAD : (h + 1) * HEAD]
                kv = lax.dot_general(
                    k, v, (((0,), (0,)), ((), ())), preferred_element_type=jnp.float32
                )
                for rb in range(per_head):
                    o_ref[h * per_head + rb, :, t * HEAD : (t + 1) * HEAD] = kv[
                        rb * rows : (rb + 1) * rows, :
                    ]

    return pl.pallas_call(
        body,
        out_shape=jax.ShapeDtypeStruct((n_dev, rows, dates * HEAD), jnp.float32),
        in_specs=[pl.BlockSpec(memory_space=pltpu.VMEM), pl.BlockSpec(memory_space=pltpu.VMEM)],
        out_specs=pl.BlockSpec(memory_space=pltpu.VMEM),
    )(key, value)


def shards(frames, cloud_mask, qkv_weight, out_weight, norm_gain, head_norm_scale, decay):
    dates_here, tokens_here, width = frames.shape
    heads = HEADS
    n_space = lax.axis_size("space")
    n_date = lax.axis_size("date")
    n_dev = n_date * n_space
    everyone = ("date", "space")
    me = lax.axis_index("date") * n_space + lax.axis_index("space")
    entries = heads * HEAD * HEAD // n_dev
    per_head = n_dev // heads
    dates_all = n_date * dates_here
    to_each = jnp.repeat(jnp.transpose(decay, (2, 0, 1)), per_head, axis=0)
    from_each = lax.all_to_all(to_each, everyone, 0, 0, tiled=True)
    my_decay = from_each.reshape(n_date, n_space, STACK_LEVELS, dates_here)[:, 0]
    my_decay = jnp.transpose(my_decay, (1, 0, 2)).reshape(STACK_LEVELS, dates_all)
    pos = jnp.arange(dates_all)
    current = frames
    flag_f = cloud_mask.astype(jnp.float32)[:, :, None]
    for layer in range(STACK_LEVELS):
        xf = current.astype(jnp.float32)
        in_msq = jnp.mean(xf * xf, -1, keepdims=True) + 1e-05
        normalized_output = (xf * lax.rsqrt(in_msq) * norm_gain[layer]).astype(jnp.bfloat16)
        flat = normalized_output.reshape(-1, width)
        proj_kv = jnp.dot(flat, qkv_weight[layer, :, width:], preferred_element_type=jnp.float32)
        proj_kv = proj_kv.reshape(dates_here, tokens_here, 2 * width)
        key = (feature(proj_kv[:, :, :width]) * flag_f).astype(jnp.bfloat16)
        value = proj_kv[:, :, width:].astype(jnp.bfloat16)
        pieces = lax.all_to_all(kv_chunks(key, value, n_dev), everyone, 0, 0, tiled=True)
        rows = pieces.shape[1]
        kv = pieces.reshape(n_date, n_space, rows, dates_here, HEAD).sum(1)
        kv = jnp.transpose(kv, (0, 2, 1, 3)).reshape(dates_all, entries)
        d = my_decay[layer]
        inside = (pos[None, None, :] > pos[None, :, None]) & (pos[None, None, :] <= pos[:, None, None])
        weight = jnp.prod(jnp.where(inside, d[None, None, :], 1.0), axis=2)
        weight = jnp.where(pos[None, :] <= pos[:, None], weight, 0.0)
        states = jnp.dot(weight, kv, precision=lax.Precision.HIGHEST, preferred_element_type=jnp.float32)
        state_b = states.astype(jnp.bfloat16).reshape(n_date, 1, dates_here, entries)
        outgoing = jnp.broadcast_to(state_b, (n_date, n_space, dates_here, entries)).reshape(
            n_dev, dates_here, entries
        )
        back = lax.all_to_all(outgoing, everyone, 0, 0, tiled=True)
        state_b = jnp.transpose(back, (1, 0, 2)).reshape(dates_here, heads, HEAD, HEAD)

        proj_q = jnp.dot(flat, qkv_weight[layer, :, :width], preferred_element_type=jnp.float32)
        query = (
            feature(proj_q)
            .astype(jnp.bfloat16)
            .reshape(dates_here, tokens_here, heads, HEAD)
        )
        numer = jnp.einsum("tshe,thef->tshf", query, state_b, preferred_element_type=jnp.float32)
        head_msq = jnp.mean(numer * numer, -1, keepdims=True) + 1e-05
        numer = numer * lax.rsqrt(head_msq)
        mixed = (numer.reshape(dates_here, tokens_here, width) * head_norm_scale[layer]).astype(
            jnp.bfloat16
        )
        update = jnp.dot(
            mixed.reshape(-1, width), out_weight[layer], preferred_element_type=jnp.float32
        )
        current = (xf + update.reshape(dates_here, tokens_here, width)).astype(jnp.bfloat16)
    return current


def solution(mesh):
    placed = (
        P("date", "space", None),
        P("date", "space"),
        P(),
        P(),
        P(),
        P(),
        P(None, "date", None),
    )
    return jax.shard_map(
        shards, mesh=mesh, in_specs=placed, out_specs=P("date", "space", None), check_vma=False
    )
```

```python
import jax
import jax.numpy as jnp
from jax import lax
from jax.experimental import pallas as pl
from jax.experimental.pallas import tpu as pltpu
from jax.sharding import PartitionSpec as P

HEADS = 16
HEAD = 64
STACK_LEVELS = 2


def feature(u):
    return jax.nn.elu(u) + 1.0


def kv_chunks(key, value, n_dev):
    dates, tokens, width = key.shape
    per_head = n_dev // HEADS
    rows = HEAD // per_head

    block = 4 * HEAD

    def body(k_ref, v_ref, o_ref):
        for t in range(dates):
            for b in range(width // block):
                k = k_ref[t, :, b * block : (b + 1) * block]
                v = v_ref[t, :, b * block : (b + 1) * block]
                kv = lax.dot_general(
                    k, v, (((0,), (0,)), ((), ())), preferred_element_type=jnp.float32
                )
                for i in range(block // HEAD):
                    h = b * (block // HEAD) + i
                    for rb in range(per_head):
                        o_ref[h * per_head + rb, :, t * HEAD : (t + 1) * HEAD] = kv[
                            i * HEAD + rb * rows : i * HEAD + (rb + 1) * rows,
                            i * HEAD : (i + 1) * HEAD,
                        ]

    return pl.pallas_call(
        body,
        out_shape=jax.ShapeDtypeStruct((n_dev, rows, dates * HEAD), jnp.float32),
        in_specs=[pl.BlockSpec(memory_space=pltpu.VMEM), pl.BlockSpec(memory_space=pltpu.VMEM)],
        out_specs=pl.BlockSpec(memory_space=pltpu.VMEM),
    )(key, value)


def shards(frames, cloud_mask, qkv_weight, out_weight, norm_gain, head_norm_scale, decay):
    dates_here, tokens_here, width = frames.shape
    heads = HEADS
    n_space = lax.axis_size("space")
    n_date = lax.axis_size("date")
    n_dev = n_date * n_space
    everyone = ("date", "space")
    me = lax.axis_index("date") * n_space + lax.axis_index("space")
    entries = heads * HEAD * HEAD // n_dev
    per_head = n_dev // heads
    dates_all = n_date * dates_here
    to_each = jnp.repeat(jnp.transpose(decay, (2, 0, 1)), per_head, axis=0)
    from_each = lax.all_to_all(to_each, everyone, 0, 0, tiled=True)
    my_decay = from_each.reshape(n_date, n_space, STACK_LEVELS, dates_here)[:, 0]
    my_decay = jnp.transpose(my_decay, (1, 0, 2)).reshape(STACK_LEVELS, dates_all)
    pos = jnp.arange(dates_all)
    current = frames
    flag_f = cloud_mask.astype(jnp.float32)[:, :, None]
    for layer in range(STACK_LEVELS):
        xf = current.astype(jnp.float32)
        in_msq = jnp.mean(xf * xf, -1, keepdims=True) + 1e-05
        normalized_output = (xf * lax.rsqrt(in_msq) * norm_gain[layer]).astype(jnp.bfloat16)
        flat = normalized_output.reshape(-1, width)
        proj_kv = jnp.dot(flat, qkv_weight[layer, :, width:], preferred_element_type=jnp.float32)
        proj_kv = proj_kv.reshape(dates_here, tokens_here, 2 * width)
        key = (feature(proj_kv[:, :, :width]) * flag_f).astype(jnp.bfloat16)
        value = proj_kv[:, :, width:].astype(jnp.bfloat16)
        pieces = lax.all_to_all(kv_chunks(key, value, n_dev), everyone, 0, 0, tiled=True)
        rows = pieces.shape[1]
        kv = pieces.reshape(n_date, n_space, rows, dates_here, HEAD).sum(1)
        kv = jnp.transpose(kv, (0, 2, 1, 3)).reshape(dates_all, entries)
        d = my_decay[layer]
        inside = (pos[None, None, :] > pos[None, :, None]) & (pos[None, None, :] <= pos[:, None, None])
        weight = jnp.prod(jnp.where(inside, d[None, None, :], 1.0), axis=2)
        weight = jnp.where(pos[None, :] <= pos[:, None], weight, 0.0)
        states = jnp.dot(weight, kv, precision=lax.Precision.HIGHEST, preferred_element_type=jnp.float32)
        state_b = states.astype(jnp.bfloat16).reshape(n_date, 1, dates_here, entries)
        outgoing = jnp.broadcast_to(state_b, (n_date, n_space, dates_here, entries)).reshape(
            n_dev, dates_here, entries
        )
        back = lax.all_to_all(outgoing, everyone, 0, 0, tiled=True)
        state_b = jnp.transpose(back, (1, 0, 2)).reshape(dates_here, heads, HEAD, HEAD)

        proj_q = jnp.dot(flat, qkv_weight[layer, :, :width], preferred_element_type=jnp.float32)
        query = (
            feature(proj_q)
            .astype(jnp.bfloat16)
            .reshape(dates_here, tokens_here, heads, HEAD)
        )
        numer = jnp.einsum("tshe,thef->tshf", query, state_b, preferred_element_type=jnp.float32)
        head_msq = jnp.mean(numer * numer, -1, keepdims=True) + 1e-05
        numer = numer * lax.rsqrt(head_msq)
        mixed = (numer.reshape(dates_here, tokens_here, width) * head_norm_scale[layer]).astype(
            jnp.bfloat16
        )
        update = jnp.dot(
            mixed.reshape(-1, width), out_weight[layer], preferred_element_type=jnp.float32
        )
        current = (xf + update.reshape(dates_here, tokens_here, width)).astype(jnp.bfloat16)
    return current


def solution(mesh):
    placed = (
        P("date", "space", None),
        P("date", "space"),
        P(),
        P(),
        P(),
        P(),
        P(None, "date", None),
    )
    return jax.shard_map(
        shards, mesh=mesh, in_specs=placed, out_specs=P("date", "space", None), check_vma=False
    )
```

```python
import jax
import jax.numpy as jnp
from jax import lax
from jax.experimental import pallas as pl
from jax.experimental.pallas import tpu as pltpu
from jax.sharding import PartitionSpec as P

HEADS = 16
HEAD = 64
STACK_LEVELS = 2


def feature(u):
    return jax.nn.elu(u) + 1.0


def kv_chunks(key, value, n_dev):
    dates, tokens, width = key.shape
    per_head = n_dev // HEADS
    rows = HEAD // per_head

    block = 4 * HEAD

    def body(k_ref, v_ref, o_ref):
        for t in range(dates):
            for b in range(width // block):
                k = k_ref[t, :, b * block : (b + 1) * block]
                v = v_ref[t, :, b * block : (b + 1) * block]
                kv = lax.dot_general(
                    k, v, (((0,), (0,)), ((), ())), preferred_element_type=jnp.float32
                )
                for i in range(block // HEAD):
                    h = b * (block // HEAD) + i
                    for rb in range(per_head):
                        o_ref[h * per_head + rb, :, t * HEAD : (t + 1) * HEAD] = kv[
                            i * HEAD + rb * rows : i * HEAD + (rb + 1) * rows,
                            i * HEAD : (i + 1) * HEAD,
                        ]

    return pl.pallas_call(
        body,
        out_shape=jax.ShapeDtypeStruct((n_dev, rows, dates * HEAD), jnp.float32),
        in_specs=[pl.BlockSpec(memory_space=pltpu.VMEM), pl.BlockSpec(memory_space=pltpu.VMEM)],
        out_specs=pl.BlockSpec(memory_space=pltpu.VMEM),
    )(key, value)


def shards(frames, cloud_mask, qkv_weight, out_weight, norm_gain, head_norm_scale, decay):
    dates_here, tokens_here, width = frames.shape
    heads = HEADS
    n_space = lax.axis_size("space")
    n_date = lax.axis_size("date")
    n_dev = n_date * n_space
    everyone = ("date", "space")
    me = lax.axis_index("date") * n_space + lax.axis_index("space")
    entries = heads * HEAD * HEAD // n_dev
    per_head = n_dev // heads
    dates_all = n_date * dates_here
    to_each = jnp.repeat(jnp.transpose(decay, (2, 0, 1)), per_head, axis=0)
    from_each = lax.all_to_all(to_each, everyone, 0, 0, tiled=True)
    my_decay = from_each.reshape(n_date, n_space, STACK_LEVELS, dates_here)[:, 0]
    my_decay = jnp.transpose(my_decay, (1, 0, 2)).reshape(STACK_LEVELS, dates_all)
    pos = jnp.arange(dates_all)
    current = frames
    flag_f = cloud_mask.astype(jnp.float32)[:, :, None]
    for layer in range(STACK_LEVELS):
        xf = current.astype(jnp.float32)
        in_msq = jnp.mean(xf * xf, -1, keepdims=True) + 1e-05
        normalized_output = (xf * lax.rsqrt(in_msq) * norm_gain[layer]).astype(jnp.bfloat16)
        flat = normalized_output.reshape(-1, width)
        proj_kv = jnp.dot(flat, qkv_weight[layer, :, width:], preferred_element_type=jnp.float32)
        proj_kv = proj_kv.reshape(dates_here, tokens_here, 2 * width)
        key = (feature(proj_kv[:, :, :width]) * flag_f).astype(jnp.bfloat16)
        value = proj_kv[:, :, width:].astype(jnp.bfloat16)
        pieces = lax.all_to_all(kv_chunks(key, value, n_dev), everyone, 0, 0, tiled=True)
        rows = pieces.shape[1]
        kv = pieces.reshape(n_date, n_space, rows, dates_here, HEAD).sum(1)
        kv = jnp.transpose(kv, (0, 2, 1, 3)).reshape(dates_all, entries)
        d = my_decay[layer]
        inside = (pos[None, None, :] > pos[None, :, None]) & (pos[None, None, :] <= pos[:, None, None])
        weight = jnp.prod(jnp.where(inside, d[None, None, :], 1.0), axis=2)
        weight = jnp.where(pos[None, :] <= pos[:, None], weight, 0.0)
        states = jnp.dot(weight, kv, precision=lax.Precision.HIGHEST, preferred_element_type=jnp.float32)
        proj_q = jnp.dot(flat, qkv_weight[layer, :, :width], preferred_element_type=jnp.float32)
        query = (
            feature(proj_q)
            .astype(jnp.bfloat16)
            .reshape(dates_here, tokens_here, heads, HEAD)
        )
        states, query = lax.optimization_barrier((states, query))
        state_b = states.astype(jnp.bfloat16).reshape(n_date, 1, dates_here, entries)
        outgoing = jnp.broadcast_to(state_b, (n_date, n_space, dates_here, entries)).reshape(
            n_dev, dates_here, entries
        )
        back = lax.all_to_all(outgoing, everyone, 0, 0, tiled=True)
        state_b = jnp.transpose(back, (1, 0, 2)).reshape(dates_here, heads, HEAD, HEAD)

        numer = jnp.einsum("tshe,thef->tshf", query, state_b, preferred_element_type=jnp.float32)
        head_msq = jnp.mean(numer * numer, -1, keepdims=True) + 1e-05
        numer = numer * lax.rsqrt(head_msq)
        mixed = (numer.reshape(dates_here, tokens_here, width) * head_norm_scale[layer]).astype(
            jnp.bfloat16
        )
        update = jnp.dot(
            mixed.reshape(-1, width), out_weight[layer], preferred_element_type=jnp.float32
        )
        current = (xf + update.reshape(dates_here, tokens_here, width)).astype(jnp.bfloat16)
    return current


def solution(mesh):
    placed = (
        P("date", "space", None),
        P("date", "space"),
        P(),
        P(),
        P(),
        P(),
        P(None, "date", None),
    )
    return jax.shard_map(
        shards, mesh=mesh, in_specs=placed, out_specs=P("date", "space", None), check_vma=False
    )
```

```python
import jax
import jax.numpy as jnp
from jax import lax
from jax.experimental import pallas as pl
from jax.experimental.pallas import tpu as pltpu
from jax.sharding import PartitionSpec as P

HEADS = 16
HEAD = 64
STACK_LEVELS = 2


def feature(u):
    return jax.nn.elu(u) + 1.0


def kv_chunks(key, value, n_dev):
    dates, tokens, width = key.shape
    per_head = n_dev // HEADS
    rows = HEAD // per_head

    block = 4 * HEAD

    def body(k_ref, v_ref, o_ref):
        for t in range(dates):
            for b in range(width // block):
                k = k_ref[t, :, b * block : (b + 1) * block]
                v = v_ref[t, :, b * block : (b + 1) * block]
                kv = lax.dot_general(
                    k, v, (((0,), (0,)), ((), ())), preferred_element_type=jnp.float32
                )
                for i in range(block // HEAD):
                    h = b * (block // HEAD) + i
                    for rb in range(per_head):
                        o_ref[h * per_head + rb, :, t * HEAD : (t + 1) * HEAD] = kv[
                            i * HEAD + rb * rows : i * HEAD + (rb + 1) * rows,
                            i * HEAD : (i + 1) * HEAD,
                        ]

    return pl.pallas_call(
        body,
        out_shape=jax.ShapeDtypeStruct((n_dev, rows, dates * HEAD), jnp.float32),
        in_specs=[pl.BlockSpec(memory_space=pltpu.VMEM), pl.BlockSpec(memory_space=pltpu.VMEM)],
        out_specs=pl.BlockSpec(memory_space=pltpu.VMEM),
    )(key, value)


def shards(frames, cloud_mask, qkv_weight, out_weight, norm_gain, head_norm_scale, decay):
    dates_here, tokens_here, width = frames.shape
    heads = HEADS
    n_space = lax.axis_size("space")
    n_date = lax.axis_size("date")
    n_dev = n_date * n_space
    everyone = ("date", "space")
    me = lax.axis_index("date") * n_space + lax.axis_index("space")
    entries = heads * HEAD * HEAD // n_dev
    per_head = n_dev // heads
    dates_all = n_date * dates_here
    to_each = jnp.repeat(jnp.transpose(decay, (2, 0, 1)), per_head, axis=0)
    from_each = lax.all_to_all(to_each, everyone, 0, 0, tiled=True)
    my_decay = from_each.reshape(n_date, n_space, STACK_LEVELS, dates_here)[:, 0]
    my_decay = jnp.transpose(my_decay, (1, 0, 2)).reshape(STACK_LEVELS, dates_all)
    pos = jnp.arange(dates_all)
    current = frames
    flag_f = cloud_mask.astype(jnp.float32)[:, :, None]
    for layer in range(STACK_LEVELS):
        xf = current.astype(jnp.float32)
        in_msq = jnp.mean(xf * xf, -1, keepdims=True) + 1e-05
        normalized_output = (xf * lax.rsqrt(in_msq) * norm_gain[layer]).astype(jnp.bfloat16)
        flat = normalized_output.reshape(-1, width)
        proj_k = jnp.dot(flat, qkv_weight[layer, :, width : 2 * width], preferred_element_type=jnp.float32)
        key = (feature(proj_k.reshape(dates_here, tokens_here, width)) * flag_f).astype(jnp.bfloat16)
        proj_v = jnp.dot(flat, qkv_weight[layer, :, 2 * width :], preferred_element_type=jnp.float32)
        value = proj_v.reshape(dates_here, tokens_here, width).astype(jnp.bfloat16)
        pieces = lax.all_to_all(kv_chunks(key, value, n_dev), everyone, 0, 0, tiled=True)
        rows = pieces.shape[1]
        kv = pieces.reshape(n_date, n_space, rows, dates_here, HEAD).sum(1)
        kv = jnp.transpose(kv, (0, 2, 1, 3)).reshape(dates_all, entries)
        d = my_decay[layer]
        inside = (pos[None, None, :] > pos[None, :, None]) & (pos[None, None, :] <= pos[:, None, None])
        weight = jnp.prod(jnp.where(inside, d[None, None, :], 1.0), axis=2)
        weight = jnp.where(pos[None, :] <= pos[:, None], weight, 0.0)
        states = jnp.dot(weight, kv, precision=lax.Precision.HIGHEST, preferred_element_type=jnp.float32)
        proj_q = jnp.dot(flat, qkv_weight[layer, :, :width], preferred_element_type=jnp.float32)
        query = (
            feature(proj_q)
            .astype(jnp.bfloat16)
            .reshape(dates_here, tokens_here, heads, HEAD)
        )
        states, query = lax.optimization_barrier((states, query))
        state_b = states.astype(jnp.bfloat16).reshape(n_date, 1, dates_here, entries)
        outgoing = jnp.broadcast_to(state_b, (n_date, n_space, dates_here, entries)).reshape(
            n_dev, dates_here, entries
        )
        back = lax.all_to_all(outgoing, everyone, 0, 0, tiled=True)
        state_b = jnp.transpose(back, (1, 0, 2)).reshape(dates_here, heads, HEAD, HEAD)

        numer = jnp.einsum("tshe,thef->tshf", query, state_b, preferred_element_type=jnp.float32)
        head_msq = jnp.mean(numer * numer, -1, keepdims=True) + 1e-05
        numer = numer * lax.rsqrt(head_msq)
        mixed = (numer.reshape(dates_here, tokens_here, width) * head_norm_scale[layer]).astype(
            jnp.bfloat16
        )
        update = jnp.dot(
            mixed.reshape(-1, width), out_weight[layer], preferred_element_type=jnp.float32
        )
        current = (xf + update.reshape(dates_here, tokens_here, width)).astype(jnp.bfloat16)
    return current


def solution(mesh):
    placed = (
        P("date", "space", None),
        P("date", "space"),
        P(),
        P(),
        P(),
        P(),
        P(None, "date", None),
    )
    return jax.shard_map(
        shards, mesh=mesh, in_specs=placed, out_specs=P("date", "space", None), check_vma=False
    )
```

```python
import jax
import jax.numpy as jnp
from jax import lax
from jax.experimental import pallas as pl
from jax.experimental.pallas import tpu as pltpu
from jax.sharding import PartitionSpec as P

HEADS = 16
HEAD = 64
STACK_LEVELS = 2


def feature(u):
    return jax.nn.elu(u) + 1.0


def kv_chunks(key, value, n_dev):
    dates, tokens, width = key.shape
    per_head = n_dev // HEADS
    rows = HEAD // per_head

    block = 4 * HEAD

    def body(k_ref, v_ref, o_ref):
        for t in range(dates):
            for b in range(width // block):
                k = k_ref[t, :, b * block : (b + 1) * block]
                v = v_ref[t, :, b * block : (b + 1) * block]
                kv = lax.dot_general(
                    k, v, (((0,), (0,)), ((), ())), preferred_element_type=jnp.float32
                )
                for i in range(block // HEAD):
                    h = b * (block // HEAD) + i
                    for rb in range(per_head):
                        o_ref[h * per_head + rb, :, t * HEAD : (t + 1) * HEAD] = kv[
                            i * HEAD + rb * rows : i * HEAD + (rb + 1) * rows,
                            i * HEAD : (i + 1) * HEAD,
                        ]

    return pl.pallas_call(
        body,
        out_shape=jax.ShapeDtypeStruct((n_dev, rows, dates * HEAD), jnp.float32),
        in_specs=[pl.BlockSpec(memory_space=pltpu.VMEM), pl.BlockSpec(memory_space=pltpu.VMEM)],
        out_specs=pl.BlockSpec(memory_space=pltpu.VMEM),
    )(key, value)


def shards(frames, cloud_mask, qkv_weight, out_weight, norm_gain, head_norm_scale, decay):
    dates_here, tokens_here, width = frames.shape
    heads = HEADS
    n_space = lax.axis_size("space")
    n_date = lax.axis_size("date")
    n_dev = n_date * n_space
    everyone = ("date", "space")
    me = lax.axis_index("date") * n_space + lax.axis_index("space")
    entries = heads * HEAD * HEAD // n_dev
    per_head = n_dev // heads
    dates_all = n_date * dates_here
    to_each = jnp.repeat(jnp.transpose(decay, (2, 0, 1)), per_head, axis=0)
    from_each = lax.all_to_all(to_each, everyone, 0, 0, tiled=True)
    my_decay = from_each.reshape(n_date, n_space, STACK_LEVELS, dates_here)[:, 0]
    my_decay = jnp.transpose(my_decay, (1, 0, 2)).reshape(STACK_LEVELS, dates_all)
    pos = jnp.arange(dates_all)
    flag_f = cloud_mask.astype(jnp.float32)[:, :, None]
    def one_layer(layer, current):
        xf = current.astype(jnp.float32)
        in_msq = jnp.mean(xf * xf, -1, keepdims=True) + 1e-05
        normalized_output = (xf * lax.rsqrt(in_msq) * norm_gain[layer]).astype(jnp.bfloat16)
        flat = normalized_output.reshape(-1, width)
        proj_k = jnp.dot(flat, qkv_weight[layer, :, width : 2 * width], preferred_element_type=jnp.float32)
        key = (feature(proj_k.reshape(dates_here, tokens_here, width)) * flag_f).astype(jnp.bfloat16)
        proj_v = jnp.dot(flat, qkv_weight[layer, :, 2 * width :], preferred_element_type=jnp.float32)
        value = proj_v.reshape(dates_here, tokens_here, width).astype(jnp.bfloat16)
        pieces = lax.all_to_all(kv_chunks(key, value, n_dev), everyone, 0, 0, tiled=True)
        rows = pieces.shape[1]
        kv = pieces.reshape(n_date, n_space, rows, dates_here, HEAD).sum(1)
        kv = jnp.transpose(kv, (0, 2, 1, 3)).reshape(dates_all, entries)
        d = my_decay[layer]
        inside = (pos[None, None, :] > pos[None, :, None]) & (pos[None, None, :] <= pos[:, None, None])
        weight = jnp.prod(jnp.where(inside, d[None, None, :], 1.0), axis=2)
        weight = jnp.where(pos[None, :] <= pos[:, None], weight, 0.0)
        states = jnp.dot(weight, kv, precision=lax.Precision.HIGHEST, preferred_element_type=jnp.float32)
        proj_q = jnp.dot(flat, qkv_weight[layer, :, :width], preferred_element_type=jnp.float32)
        query = (
            feature(proj_q)
            .astype(jnp.bfloat16)
            .reshape(dates_here, tokens_here, heads, HEAD)
        )
        states, query = lax.optimization_barrier((states, query))
        state_b = states.astype(jnp.bfloat16).reshape(n_date, 1, dates_here, entries)
        outgoing = jnp.broadcast_to(state_b, (n_date, n_space, dates_here, entries)).reshape(
            n_dev, dates_here, entries
        )
        back = lax.all_to_all(outgoing, everyone, 0, 0, tiled=True)
        state_b = jnp.transpose(back, (1, 0, 2)).reshape(dates_here, heads, HEAD, HEAD)

        numer = jnp.einsum("tshe,thef->tshf", query, state_b, preferred_element_type=jnp.float32)
        head_msq = jnp.mean(numer * numer, -1, keepdims=True) + 1e-05
        numer = numer * lax.rsqrt(head_msq)
        mixed = (numer.reshape(dates_here, tokens_here, width) * head_norm_scale[layer]).astype(
            jnp.bfloat16
        )
        update = jnp.dot(
            mixed.reshape(-1, width), out_weight[layer], preferred_element_type=jnp.float32
        )
        return (xf + update.reshape(dates_here, tokens_here, width)).astype(jnp.bfloat16)

    return lax.fori_loop(0, STACK_LEVELS, one_layer, frames)


def solution(mesh):
    placed = (
        P("date", "space", None),
        P("date", "space"),
        P(),
        P(),
        P(),
        P(),
        P(None, "date", None),
    )
    return jax.shard_map(
        shards, mesh=mesh, in_specs=placed, out_specs=P("date", "space", None), check_vma=False
    )
```

```python
import jax
import jax.numpy as jnp
from jax import lax
from jax.experimental import pallas as pl
from jax.experimental.pallas import tpu as pltpu
from jax.sharding import PartitionSpec as P

HEADS = 16
HEAD = 64
STACK_LEVELS = 2


def feature(u):
    return jax.nn.elu(u) + 1.0


def kv_chunks(key, value, extra, n_dev):
    dates, tokens, width = key.shape
    per_head = n_dev // HEADS
    rows = HEAD // per_head

    block = 4 * HEAD

    def body(k_ref, v_ref, e_ref, o_ref):
        o_ref[:, :, dates * HEAD :] = e_ref[...]
        for t in range(dates):
            for b in range(width // block):
                k = k_ref[t, :, b * block : (b + 1) * block]
                v = v_ref[t, :, b * block : (b + 1) * block]
                kv = lax.dot_general(
                    k, v, (((0,), (0,)), ((), ())), preferred_element_type=jnp.float32
                )
                for i in range(block // HEAD):
                    h = b * (block // HEAD) + i
                    for rb in range(per_head):
                        o_ref[h * per_head + rb, :, t * HEAD : (t + 1) * HEAD] = kv[
                            i * HEAD + rb * rows : i * HEAD + (rb + 1) * rows,
                            i * HEAD : (i + 1) * HEAD,
                        ]

    return pl.pallas_call(
        body,
        out_shape=jax.ShapeDtypeStruct(
            (n_dev, rows, dates * HEAD + extra.shape[2]), jnp.float32
        ),
        in_specs=[pl.BlockSpec(memory_space=pltpu.VMEM)] * 3,
        out_specs=pl.BlockSpec(memory_space=pltpu.VMEM),
    )(key, value, extra)


def shards(frames, cloud_mask, qkv_weight, out_weight, norm_gain, head_norm_scale, decay):
    dates_here, tokens_here, width = frames.shape
    heads = HEADS
    n_space = lax.axis_size("space")
    n_date = lax.axis_size("date")
    n_dev = n_date * n_space
    everyone = ("date", "space")
    me = lax.axis_index("date") * n_space + lax.axis_index("space")
    entries = heads * HEAD * HEAD // n_dev
    per_head = n_dev // heads
    dates_all = n_date * dates_here
    lanes = 128
    to_each = jnp.repeat(jnp.transpose(decay, (0, 2, 1)), per_head, axis=1)
    to_each = jnp.pad(to_each[:, :, None, :], ((0, 0), (0, 0), (0, 0), (0, lanes - dates_here)))
    pos = jnp.arange(dates_all)
    flag_f = cloud_mask.astype(jnp.float32)[:, :, None]
    def one_layer(layer, current):
        xf = current.astype(jnp.float32)
        in_msq = jnp.mean(xf * xf, -1, keepdims=True) + 1e-05
        normalized_output = (xf * lax.rsqrt(in_msq) * norm_gain[layer]).astype(jnp.bfloat16)
        flat = normalized_output.reshape(-1, width)
        proj_k = jnp.dot(flat, qkv_weight[layer, :, width : 2 * width], preferred_element_type=jnp.float32)
        key = (feature(proj_k.reshape(dates_here, tokens_here, width)) * flag_f).astype(jnp.bfloat16)
        proj_v = jnp.dot(flat, qkv_weight[layer, :, 2 * width :], preferred_element_type=jnp.float32)
        value = proj_v.reshape(dates_here, tokens_here, width).astype(jnp.bfloat16)
        extra = jnp.broadcast_to(to_each[layer], (n_dev, HEAD // per_head, lanes))
        pieces = lax.all_to_all(kv_chunks(key, value, extra, n_dev), everyone, 0, 0, tiled=True)
        rows = pieces.shape[1]
        d = pieces[:, 0, dates_here * HEAD : dates_here * HEAD + dates_here]
        d = d.reshape(n_date, n_space, dates_here)[:, 0].reshape(dates_all)
        pieces = pieces[:, :, : dates_here * HEAD]
        kv = pieces.reshape(n_date, n_space, rows, dates_here, HEAD).sum(1)
        kv = jnp.transpose(kv, (0, 2, 1, 3)).reshape(dates_all, entries)
        inside = (pos[None, None, :] > pos[None, :, None]) & (pos[None, None, :] <= pos[:, None, None])
        weight = jnp.prod(jnp.where(inside, d[None, None, :], 1.0), axis=2)
        weight = jnp.where(pos[None, :] <= pos[:, None], weight, 0.0)
        states = jnp.dot(weight, kv, precision=lax.Precision.HIGHEST, preferred_element_type=jnp.float32)
        proj_q = jnp.dot(flat, qkv_weight[layer, :, :width], preferred_element_type=jnp.float32)
        query = (
            feature(proj_q)
            .astype(jnp.bfloat16)
            .reshape(dates_here, tokens_here, heads, HEAD)
        )
        states, query = lax.optimization_barrier((states, query))
        state_b = states.astype(jnp.bfloat16).reshape(n_date, 1, dates_here, entries)
        outgoing = jnp.broadcast_to(state_b, (n_date, n_space, dates_here, entries)).reshape(
            n_dev, dates_here, entries
        )
        back = lax.all_to_all(outgoing, everyone, 0, 0, tiled=True)
        state_b = jnp.transpose(back, (1, 0, 2)).reshape(dates_here, heads, HEAD, HEAD)

        numer = jnp.einsum("tshe,thef->tshf", query, state_b, preferred_element_type=jnp.float32)
        head_msq = jnp.mean(numer * numer, -1, keepdims=True) + 1e-05
        numer = numer * lax.rsqrt(head_msq)
        mixed = (numer.reshape(dates_here, tokens_here, width) * head_norm_scale[layer]).astype(
            jnp.bfloat16
        )
        update = jnp.dot(
            mixed.reshape(-1, width), out_weight[layer], preferred_element_type=jnp.float32
        )
        return (xf + update.reshape(dates_here, tokens_here, width)).astype(jnp.bfloat16)

    return lax.fori_loop(0, STACK_LEVELS, one_layer, frames)


def solution(mesh):
    placed = (
        P("date", "space", None),
        P("date", "space"),
        P(),
        P(),
        P(),
        P(),
        P(None, "date", None),
    )
    return jax.shard_map(
        shards, mesh=mesh, in_specs=placed, out_specs=P("date", "space", None), check_vma=False
    )
```

```python
import jax
import jax.numpy as jnp
from jax import lax
from jax.experimental import pallas as pl
from jax.experimental.pallas import tpu as pltpu
from jax.sharding import PartitionSpec as P

HEADS = 16
HEAD = 64
STACK_LEVELS = 2


def feature(u):
    return jax.nn.elu(u) + 1.0


def kv_chunks(normed, flags, weights, layer, n_dev):
    dates, tokens, width = normed.shape
    per_head = n_dev // HEADS
    rows = HEAD // per_head
    block = 4 * HEAD

    def body(x_ref, m_ref, wk_ref, wv_ref, o_ref):
        t = pl.program_id(0)
        x = x_ref[0]
        u = jnp.dot(x, wk_ref[0], preferred_element_type=jnp.float32)
        key = jnp.where(u > 0, u + 1.0, jnp.exp(jnp.minimum(u, 0.0))) * m_ref[0]
        key = key.astype(jnp.bfloat16)
        value = jnp.dot(x, wv_ref[0], preferred_element_type=jnp.float32).astype(jnp.bfloat16)
        blocks = [
            lax.dot_general(
                key[:, b * block : (b + 1) * block],
                value[:, b * block : (b + 1) * block],
                (((0,), (0,)), ((), ())),
                preferred_element_type=jnp.float32,
            )
            for b in range(width // block)
        ]
        for date in range(dates):

            @pl.when(t == date)
            def _():
                for b, kv in enumerate(blocks):
                    for i in range(block // HEAD):
                        h = b * (block // HEAD) + i
                        for rb in range(per_head):
                            o_ref[h * per_head + rb, :, date * HEAD : (date + 1) * HEAD] = kv[
                                i * HEAD + rb * rows : i * HEAD + (rb + 1) * rows,
                                i * HEAD : (i + 1) * HEAD,
                            ]

    return pl.pallas_call(
        body,
        grid=(dates,),
        out_shape=jax.ShapeDtypeStruct((n_dev, rows, dates * HEAD), jnp.float32),
        in_specs=[
            pl.BlockSpec((1, tokens, width), lambda t: (t, 0, 0)),
            pl.BlockSpec((1, tokens, 1), lambda t: (t, 0, 0)),
            pl.BlockSpec((1, width, width), lambda t: (layer, 0, 1)),
            pl.BlockSpec((1, width, width), lambda t: (layer, 0, 2)),
        ],
        out_specs=pl.BlockSpec((n_dev, rows, dates * HEAD), lambda t: (0, 0, 0)),
        compiler_params=pltpu.CompilerParams(dimension_semantics=("arbitrary",)),
    )(normed, flags, weights, weights)


def shards(frames, cloud_mask, qkv_weight, out_weight, norm_gain, head_norm_scale, decay):
    dates_here, tokens_here, width = frames.shape
    heads = HEADS
    n_space = lax.axis_size("space")
    n_date = lax.axis_size("date")
    n_dev = n_date * n_space
    everyone = ("date", "space")
    me = lax.axis_index("date") * n_space + lax.axis_index("space")
    entries = heads * HEAD * HEAD // n_dev
    per_head = n_dev // heads
    dates_all = n_date * dates_here
    to_each = jnp.repeat(jnp.transpose(decay, (2, 0, 1)), per_head, axis=0)
    from_each = lax.all_to_all(to_each, everyone, 0, 0, tiled=True)
    my_decay = from_each.reshape(n_date, n_space, STACK_LEVELS, dates_here)[:, 0]
    my_decay = jnp.transpose(my_decay, (1, 0, 2)).reshape(STACK_LEVELS, dates_all)
    pos = jnp.arange(dates_all)
    current = frames
    flag_f = cloud_mask.astype(jnp.float32)[:, :, None]
    for layer in range(STACK_LEVELS):
        xf = current.astype(jnp.float32)
        in_msq = jnp.mean(xf * xf, -1, keepdims=True) + 1e-05
        normalized_output = (xf * lax.rsqrt(in_msq) * norm_gain[layer]).astype(jnp.bfloat16)
        flat = normalized_output.reshape(-1, width)
        pieces = lax.all_to_all(
            kv_chunks(normalized_output, flag_f, qkv_weight, layer, n_dev), everyone, 0, 0, tiled=True
        )
        rows = pieces.shape[1]
        kv = pieces.reshape(n_date, n_space, rows, dates_here, HEAD).sum(1)
        kv = jnp.transpose(kv, (0, 2, 1, 3)).reshape(dates_all, entries)
        d = my_decay[layer]
        inside = (pos[None, None, :] > pos[None, :, None]) & (pos[None, None, :] <= pos[:, None, None])
        weight = jnp.prod(jnp.where(inside, d[None, None, :], 1.0), axis=2)
        weight = jnp.where(pos[None, :] <= pos[:, None], weight, 0.0)
        states = jnp.dot(weight, kv, precision=lax.Precision.HIGHEST, preferred_element_type=jnp.float32)
        proj_q = jnp.dot(flat, qkv_weight[layer, :, :width], preferred_element_type=jnp.float32)
        query = (
            feature(proj_q)
            .astype(jnp.bfloat16)
            .reshape(dates_here, tokens_here, heads, HEAD)
        )
        states, query = lax.optimization_barrier((states, query))
        state_b = states.astype(jnp.bfloat16).reshape(n_date, 1, dates_here, entries)
        outgoing = jnp.broadcast_to(state_b, (n_date, n_space, dates_here, entries)).reshape(
            n_dev, dates_here, entries
        )
        back = lax.all_to_all(outgoing, everyone, 0, 0, tiled=True)
        state_b = jnp.transpose(back, (1, 0, 2)).reshape(dates_here, heads, HEAD, HEAD)

        numer = jnp.einsum("tshe,thef->tshf", query, state_b, preferred_element_type=jnp.float32)
        head_msq = jnp.mean(numer * numer, -1, keepdims=True) + 1e-05
        numer = numer * lax.rsqrt(head_msq)
        mixed = (numer.reshape(dates_here, tokens_here, width) * head_norm_scale[layer]).astype(
            jnp.bfloat16
        )
        update = jnp.dot(
            mixed.reshape(-1, width), out_weight[layer], preferred_element_type=jnp.float32
        )
        current = (xf + update.reshape(dates_here, tokens_here, width)).astype(jnp.bfloat16)
    return current


def solution(mesh):
    placed = (
        P("date", "space", None),
        P("date", "space"),
        P(),
        P(),
        P(),
        P(),
        P(None, "date", None),
    )
    return jax.shard_map(
        shards, mesh=mesh, in_specs=placed, out_specs=P("date", "space", None), check_vma=False
    )
```

```python
import jax
import jax.numpy as jnp
from jax import lax
from jax.experimental import pallas as pl
from jax.experimental.pallas import tpu as pltpu
from jax.sharding import PartitionSpec as P

HEADS = 16
HEAD = 64
STACK_LEVELS = 2


def feature(u):
    return jax.nn.elu(u) + 1.0


def kv_chunks(normed, flags, weights, layer, n_dev):
    dates, tokens, width = normed.shape
    per_head = n_dev // HEADS
    rows = HEAD // per_head
    block = 4 * HEAD

    def body(x_ref, m_ref, wk_ref, wv_ref, o_ref):
        t = pl.program_id(0)
        x = x_ref[0]
        u = jnp.dot(x, wk_ref[0], preferred_element_type=jnp.float32)
        key = jnp.where(u > 0, u + 1.0, jnp.exp(jnp.minimum(u, 0.0))) * m_ref[0]
        key = key.astype(jnp.bfloat16)
        value = jnp.dot(x, wv_ref[0], preferred_element_type=jnp.float32).astype(jnp.bfloat16)
        blocks = [
            lax.dot_general(
                key[:, b * block : (b + 1) * block],
                value[:, b * block : (b + 1) * block],
                (((0,), (0,)), ((), ())),
                preferred_element_type=jnp.float32,
            )
            for b in range(width // block)
        ]
        for date in range(dates):

            @pl.when(t == date)
            def _():
                for b, kv in enumerate(blocks):
                    for i in range(block // HEAD):
                        h = b * (block // HEAD) + i
                        for rb in range(per_head):
                            o_ref[h * per_head + rb, :, date * HEAD : (date + 1) * HEAD] = kv[
                                i * HEAD + rb * rows : i * HEAD + (rb + 1) * rows,
                                i * HEAD : (i + 1) * HEAD,
                            ]

    return pl.pallas_call(
        body,
        grid=(dates,),
        out_shape=jax.ShapeDtypeStruct((n_dev, rows, dates * HEAD), jnp.float32),
        in_specs=[
            pl.BlockSpec((1, tokens, width), lambda t: (t, 0, 0)),
            pl.BlockSpec((1, tokens, 1), lambda t: (t, 0, 0)),
            pl.BlockSpec((1, width, width), lambda t: (layer, 0, 1)),
            pl.BlockSpec((1, width, width), lambda t: (layer, 0, 2)),
        ],
        out_specs=pl.BlockSpec((n_dev, rows, dates * HEAD), lambda t: (0, 0, 0)),
        compiler_params=pltpu.CompilerParams(dimension_semantics=("arbitrary",)),
    )(normed, flags, weights, weights)


def mix_out(query, diag, scale, current, weights, layer):
    dates, tokens, width = query.shape
    block = diag.shape[-1]

    def body(q_ref, d_ref, s_ref, x_ref, w_ref, o_ref, m_ref):
        for b in range(width // block):
            numer = jnp.dot(
                q_ref[0, :, b * block : (b + 1) * block], d_ref[0, b],
                preferred_element_type=jnp.float32,
            )
            for i in range(block // HEAD):
                part = numer[:, i * HEAD : (i + 1) * HEAD]
                msq = jnp.mean(part * part, axis=-1, keepdims=True) + 1e-05
                lo = b * block + i * HEAD
                m_ref[:, lo : lo + HEAD] = (
                    part * lax.rsqrt(msq) * s_ref[:, lo : lo + HEAD]
                ).astype(jnp.bfloat16)
        update = jnp.dot(m_ref[...], w_ref[0], preferred_element_type=jnp.float32)
        o_ref[0] = (x_ref[0].astype(jnp.float32) + update).astype(jnp.bfloat16)

    return pl.pallas_call(
        body,
        grid=(dates,),
        out_shape=jax.ShapeDtypeStruct((dates, tokens, width), jnp.bfloat16),
        in_specs=[
            pl.BlockSpec((1, tokens, width), lambda t: (t, 0, 0)),
            pl.BlockSpec((1, width // block, block, block), lambda t: (t, 0, 0, 0)),
            pl.BlockSpec((1, width), lambda t: (0, 0)),
            pl.BlockSpec((1, tokens, width), lambda t: (t, 0, 0)),
            pl.BlockSpec((1, width, width), lambda t: (layer, 0, 0)),
        ],
        out_specs=pl.BlockSpec((1, tokens, width), lambda t: (t, 0, 0)),
        scratch_shapes=[pltpu.VMEM((tokens, width), jnp.bfloat16)],
        compiler_params=pltpu.CompilerParams(dimension_semantics=("arbitrary",)),
    )(query, diag, scale, current, weights)


def shards(frames, cloud_mask, qkv_weight, out_weight, norm_gain, head_norm_scale, decay):
    dates_here, tokens_here, width = frames.shape
    heads = HEADS
    n_space = lax.axis_size("space")
    n_date = lax.axis_size("date")
    n_dev = n_date * n_space
    everyone = ("date", "space")
    me = lax.axis_index("date") * n_space + lax.axis_index("space")
    entries = heads * HEAD * HEAD // n_dev
    per_head = n_dev // heads
    dates_all = n_date * dates_here
    to_each = jnp.repeat(jnp.transpose(decay, (2, 0, 1)), per_head, axis=0)
    from_each = lax.all_to_all(to_each, everyone, 0, 0, tiled=True)
    my_decay = from_each.reshape(n_date, n_space, STACK_LEVELS, dates_here)[:, 0]
    my_decay = jnp.transpose(my_decay, (1, 0, 2)).reshape(STACK_LEVELS, dates_all)
    pos = jnp.arange(dates_all)
    current = frames
    flag_f = cloud_mask.astype(jnp.float32)[:, :, None]
    for layer in range(STACK_LEVELS):
        xf = current.astype(jnp.float32)
        in_msq = jnp.mean(xf * xf, -1, keepdims=True) + 1e-05
        normalized_output = (xf * lax.rsqrt(in_msq) * norm_gain[layer]).astype(jnp.bfloat16)
        flat = normalized_output.reshape(-1, width)
        pieces = lax.all_to_all(
            kv_chunks(normalized_output, flag_f, qkv_weight, layer, n_dev), everyone, 0, 0, tiled=True
        )
        rows = pieces.shape[1]
        kv = pieces.reshape(n_date, n_space, rows, dates_here, HEAD).sum(1)
        kv = jnp.transpose(kv, (0, 2, 1, 3)).reshape(dates_all, entries)
        d = my_decay[layer]
        inside = (pos[None, None, :] > pos[None, :, None]) & (pos[None, None, :] <= pos[:, None, None])
        weight = jnp.prod(jnp.where(inside, d[None, None, :], 1.0), axis=2)
        weight = jnp.where(pos[None, :] <= pos[:, None], weight, 0.0)
        states = jnp.dot(weight, kv, precision=lax.Precision.HIGHEST, preferred_element_type=jnp.float32)
        proj_q = jnp.dot(flat, qkv_weight[layer, :, :width], preferred_element_type=jnp.float32)
        query = (
            feature(proj_q)
            .astype(jnp.bfloat16)
            .reshape(dates_here, tokens_here, heads, HEAD)
        )
        states, query = lax.optimization_barrier((states, query))
        state_b = states.astype(jnp.bfloat16).reshape(n_date, 1, dates_here, entries)
        outgoing = jnp.broadcast_to(state_b, (n_date, n_space, dates_here, entries)).reshape(
            n_dev, dates_here, entries
        )
        back = lax.all_to_all(outgoing, everyone, 0, 0, tiled=True)
        state_b = jnp.transpose(back, (1, 0, 2)).reshape(dates_here, heads, HEAD, HEAD)

        per = 4
        tiles = state_b.reshape(dates_here, heads // per, per, HEAD, HEAD)
        eye = jnp.eye(per, dtype=jnp.bfloat16)
        diag = jnp.einsum("tbief,ij->tbiejf", tiles, eye).reshape(
            dates_here, heads // per, per * HEAD, per * HEAD
        )
        current = mix_out(
            query.reshape(dates_here, tokens_here, width), diag, head_norm_scale[layer][None, :], current,
            out_weight, layer,
        )
    return current


def solution(mesh):
    placed = (
        P("date", "space", None),
        P("date", "space"),
        P(),
        P(),
        P(),
        P(),
        P(None, "date", None),
    )
    return jax.shard_map(
        shards, mesh=mesh, in_specs=placed, out_specs=P("date", "space", None), check_vma=False
    )
```

```python
import jax
import jax.numpy as jnp
from jax import lax
from jax.experimental import pallas as pl
from jax.experimental.pallas import tpu as pltpu
from jax.sharding import PartitionSpec as P

HEADS = 16
HEAD = 64
STACK_LEVELS = 2


def feature(u):
    return jax.nn.elu(u) + 1.0


def kv_chunks(normed, flags, weights, layer, n_dev):
    dates, tokens, width = normed.shape
    per_head = n_dev // HEADS
    rows = HEAD // per_head
    block = 4 * HEAD

    def body(x_ref, m_ref, wk_ref, wv_ref, o_ref):
        t = pl.program_id(0)
        x = x_ref[0]
        u = jnp.dot(x, wk_ref[0], preferred_element_type=jnp.float32)
        key = jnp.where(u > 0, u + 1.0, jnp.exp(jnp.minimum(u, 0.0))) * m_ref[0]
        key = key.astype(jnp.bfloat16)
        value = jnp.dot(x, wv_ref[0], preferred_element_type=jnp.float32).astype(jnp.bfloat16)
        blocks = [
            lax.dot_general(
                key[:, b * block : (b + 1) * block],
                value[:, b * block : (b + 1) * block],
                (((0,), (0,)), ((), ())),
                preferred_element_type=jnp.float32,
            )
            for b in range(width // block)
        ]
        for date in range(dates):

            @pl.when(t == date)
            def _():
                for b, kv in enumerate(blocks):
                    for i in range(block // HEAD):
                        h = b * (block // HEAD) + i
                        for rb in range(per_head):
                            o_ref[h * per_head + rb, :, date * HEAD : (date + 1) * HEAD] = kv[
                                i * HEAD + rb * rows : i * HEAD + (rb + 1) * rows,
                                i * HEAD : (i + 1) * HEAD,
                            ]

    return pl.pallas_call(
        body,
        grid=(dates,),
        out_shape=jax.ShapeDtypeStruct((n_dev, rows, dates * HEAD), jnp.float32),
        in_specs=[
            pl.BlockSpec((1, tokens, width), lambda t: (t, 0, 0)),
            pl.BlockSpec((1, tokens, 1), lambda t: (t, 0, 0)),
            pl.BlockSpec((1, width, width), lambda t: (layer, 0, 1)),
            pl.BlockSpec((1, width, width), lambda t: (layer, 0, 2)),
        ],
        out_specs=pl.BlockSpec((n_dev, rows, dates * HEAD), lambda t: (0, 0, 0)),
        compiler_params=pltpu.CompilerParams(dimension_semantics=("arbitrary",)),
    )(normed, flags, weights, weights)


def shards(frames, cloud_mask, qkv_weight, out_weight, norm_gain, head_norm_scale, decay):
    dates_here, tokens_here, width = frames.shape
    heads = HEADS
    n_space = lax.axis_size("space")
    n_date = lax.axis_size("date")
    n_dev = n_date * n_space
    everyone = ("date", "space")
    me = lax.axis_index("date") * n_space + lax.axis_index("space")
    entries = heads * HEAD * HEAD // n_dev
    per_head = n_dev // heads
    dates_all = n_date * dates_here
    to_each = jnp.repeat(jnp.transpose(decay, (2, 0, 1)), per_head, axis=0)
    from_each = lax.all_to_all(to_each, everyone, 0, 0, tiled=True)
    my_decay = from_each.reshape(n_date, n_space, STACK_LEVELS, dates_here)[:, 0]
    my_decay = jnp.transpose(my_decay, (1, 0, 2)).reshape(STACK_LEVELS, dates_all)
    pos = jnp.arange(dates_all)
    current = frames
    flag_f = cloud_mask.astype(jnp.float32)[:, :, None]
    for layer in range(STACK_LEVELS):
        xf = current.astype(jnp.float32)
        in_msq = jnp.mean(xf * xf, -1, keepdims=True) + 1e-05
        normalized_output = (xf * lax.rsqrt(in_msq) * norm_gain[layer]).astype(jnp.bfloat16)
        flat = normalized_output.reshape(-1, width)
        pieces = lax.all_to_all(
            kv_chunks(normalized_output, flag_f, qkv_weight, layer, n_dev), everyone, 0, 0, tiled=True
        )
        rows = pieces.shape[1]
        kv = pieces.reshape(n_date, n_space, rows, dates_here * HEAD).sum(1)
        kv = lax.optimization_barrier(kv).reshape(n_date, rows, dates_here, HEAD)
        kv = jnp.transpose(kv, (0, 2, 1, 3)).reshape(dates_all, entries)
        d = my_decay[layer]
        inside = (pos[None, None, :] > pos[None, :, None]) & (pos[None, None, :] <= pos[:, None, None])
        weight = jnp.prod(jnp.where(inside, d[None, None, :], 1.0), axis=2)
        weight = jnp.where(pos[None, :] <= pos[:, None], weight, 0.0)
        states = jnp.dot(weight, kv, precision=lax.Precision.HIGHEST, preferred_element_type=jnp.float32)
        proj_q = jnp.dot(flat, qkv_weight[layer, :, :width], preferred_element_type=jnp.float32)
        query = (
            feature(proj_q)
            .astype(jnp.bfloat16)
            .reshape(dates_here, tokens_here, heads, HEAD)
        )
        states, query = lax.optimization_barrier((states, query))
        state_b = states.astype(jnp.bfloat16).reshape(n_date, 1, dates_here, entries)
        outgoing = jnp.broadcast_to(state_b, (n_date, n_space, dates_here, entries)).reshape(
            n_dev, dates_here, entries
        )
        back = lax.all_to_all(outgoing, everyone, 0, 0, tiled=True)
        state_b = jnp.transpose(back, (1, 0, 2)).reshape(dates_here, heads, HEAD, HEAD)

        numer = jnp.einsum("tshe,thef->tshf", query, state_b, preferred_element_type=jnp.float32)
        head_msq = jnp.mean(numer * numer, -1, keepdims=True) + 1e-05
        numer = numer * lax.rsqrt(head_msq)
        mixed = (numer.reshape(dates_here, tokens_here, width) * head_norm_scale[layer]).astype(
            jnp.bfloat16
        )
        update = jnp.dot(
            mixed.reshape(-1, width), out_weight[layer], preferred_element_type=jnp.float32
        )
        current = (xf + update.reshape(dates_here, tokens_here, width)).astype(jnp.bfloat16)
    return current


def solution(mesh):
    placed = (
        P("date", "space", None),
        P("date", "space"),
        P(),
        P(),
        P(),
        P(),
        P(None, "date", None),
    )
    return jax.shard_map(
        shards, mesh=mesh, in_specs=placed, out_specs=P("date", "space", None), check_vma=False
    )
```

```python
import jax
import jax.numpy as jnp
from jax import lax
from jax.experimental import pallas as pl
from jax.experimental.pallas import tpu as pltpu
from jax.sharding import PartitionSpec as P

HEADS = 16
HEAD = 64
STACK_LEVELS = 2


def feature(u):
    return jax.nn.elu(u) + 1.0


def kv_chunks(normed, flags, weights, layer, n_dev):
    dates, tokens, width = normed.shape
    per_head = n_dev // HEADS
    rows = HEAD // per_head
    block = 4 * HEAD

    step = 2

    def body(x_ref, m_ref, wk_ref, wv_ref, o_ref):
        t = pl.program_id(0)
        x = x_ref[...].reshape(step * tokens, width)
        u = jnp.dot(x, wk_ref[0], preferred_element_type=jnp.float32)
        key = jnp.where(u > 0, u + 1.0, jnp.exp(jnp.minimum(u, 0.0))) * m_ref[...].reshape(step * tokens, 1)
        key = key.astype(jnp.bfloat16)
        value = jnp.dot(x, wv_ref[0], preferred_element_type=jnp.float32).astype(jnp.bfloat16)
        for sub in range(step):
            rows_of = slice(sub * tokens, (sub + 1) * tokens)
            blocks = [
                lax.dot_general(
                    key[rows_of, b * block : (b + 1) * block],
                    value[rows_of, b * block : (b + 1) * block],
                    (((0,), (0,)), ((), ())),
                    preferred_element_type=jnp.float32,
                )
                for b in range(width // block)
            ]
            for first in range(0, dates, step):

                @pl.when(t * step == first)
                def _():
                    date = first + sub
                    for b, kv in enumerate(blocks):
                        for i in range(block // HEAD):
                            h = b * (block // HEAD) + i
                            for rb in range(per_head):
                                o_ref[h * per_head + rb, :, date * HEAD : (date + 1) * HEAD] = kv[
                                    i * HEAD + rb * rows : i * HEAD + (rb + 1) * rows,
                                    i * HEAD : (i + 1) * HEAD,
                                ]

    return pl.pallas_call(
        body,
        grid=(dates // step,),
        out_shape=jax.ShapeDtypeStruct((n_dev, rows, dates * HEAD), jnp.float32),
        in_specs=[
            pl.BlockSpec((step, tokens, width), lambda t: (t, 0, 0)),
            pl.BlockSpec((step, tokens, 1), lambda t: (t, 0, 0)),
            pl.BlockSpec((1, width, width), lambda t: (layer, 0, 1)),
            pl.BlockSpec((1, width, width), lambda t: (layer, 0, 2)),
        ],
        out_specs=pl.BlockSpec((n_dev, rows, dates * HEAD), lambda t: (0, 0, 0)),
        compiler_params=pltpu.CompilerParams(dimension_semantics=("arbitrary",)),
    )(normed, flags, weights, weights)


def shards(frames, cloud_mask, qkv_weight, out_weight, norm_gain, head_norm_scale, decay):
    dates_here, tokens_here, width = frames.shape
    heads = HEADS
    n_space = lax.axis_size("space")
    n_date = lax.axis_size("date")
    n_dev = n_date * n_space
    everyone = ("date", "space")
    me = lax.axis_index("date") * n_space + lax.axis_index("space")
    entries = heads * HEAD * HEAD // n_dev
    per_head = n_dev // heads
    dates_all = n_date * dates_here
    to_each = jnp.repeat(jnp.transpose(decay, (2, 0, 1)), per_head, axis=0)
    from_each = lax.all_to_all(to_each, everyone, 0, 0, tiled=True)
    my_decay = from_each.reshape(n_date, n_space, STACK_LEVELS, dates_here)[:, 0]
    my_decay = jnp.transpose(my_decay, (1, 0, 2)).reshape(STACK_LEVELS, dates_all)
    pos = jnp.arange(dates_all)
    current = frames
    flag_f = cloud_mask.astype(jnp.float32)[:, :, None]
    for layer in range(STACK_LEVELS):
        xf = current.astype(jnp.float32)
        in_msq = jnp.mean(xf * xf, -1, keepdims=True) + 1e-05
        normalized_output = (xf * lax.rsqrt(in_msq) * norm_gain[layer]).astype(jnp.bfloat16)
        flat = normalized_output.reshape(-1, width)
        pieces = lax.all_to_all(
            kv_chunks(normalized_output, flag_f, qkv_weight, layer, n_dev), everyone, 0, 0, tiled=True
        )
        rows = pieces.shape[1]
        kv = pieces.reshape(n_date, n_space, rows, dates_here * HEAD).sum(1)
        kv = lax.optimization_barrier(kv).reshape(n_date, rows, dates_here, HEAD)
        kv = jnp.transpose(kv, (0, 2, 1, 3)).reshape(dates_all, entries)
        d = my_decay[layer]
        inside = (pos[None, None, :] > pos[None, :, None]) & (pos[None, None, :] <= pos[:, None, None])
        weight = jnp.prod(jnp.where(inside, d[None, None, :], 1.0), axis=2)
        weight = jnp.where(pos[None, :] <= pos[:, None], weight, 0.0)
        states = jnp.dot(weight, kv, precision=lax.Precision.HIGHEST, preferred_element_type=jnp.float32)
        proj_q = jnp.dot(flat, qkv_weight[layer, :, :width], preferred_element_type=jnp.float32)
        query = (
            feature(proj_q)
            .astype(jnp.bfloat16)
            .reshape(dates_here, tokens_here, heads, HEAD)
        )
        states, query = lax.optimization_barrier((states, query))
        state_b = states.astype(jnp.bfloat16).reshape(n_date, 1, dates_here, entries)
        outgoing = jnp.broadcast_to(state_b, (n_date, n_space, dates_here, entries)).reshape(
            n_dev, dates_here, entries
        )
        back = lax.all_to_all(outgoing, everyone, 0, 0, tiled=True)
        state_b = jnp.transpose(back, (1, 0, 2)).reshape(dates_here, heads, HEAD, HEAD)

        numer = jnp.einsum("tshe,thef->tshf", query, state_b, preferred_element_type=jnp.float32)
        head_msq = jnp.mean(numer * numer, -1, keepdims=True) + 1e-05
        numer = numer * lax.rsqrt(head_msq)
        mixed = (numer.reshape(dates_here, tokens_here, width) * head_norm_scale[layer]).astype(
            jnp.bfloat16
        )
        update = jnp.dot(
            mixed.reshape(-1, width), out_weight[layer], preferred_element_type=jnp.float32
        )
        current = (xf + update.reshape(dates_here, tokens_here, width)).astype(jnp.bfloat16)
    return current


def solution(mesh):
    placed = (
        P("date", "space", None),
        P("date", "space"),
        P(),
        P(),
        P(),
        P(),
        P(None, "date", None),
    )
    return jax.shard_map(
        shards, mesh=mesh, in_specs=placed, out_specs=P("date", "space", None), check_vma=False
    )
```

```python
import jax
import jax.numpy as jnp
from jax import lax
from jax.experimental import pallas as pl
from jax.experimental.pallas import tpu as pltpu
from jax.sharding import PartitionSpec as P

HEADS = 16
HEAD = 64
STACK_LEVELS = 2


def feature(u):
    return jax.nn.elu(u) + 1.0


def kv_chunks(tokens_in, gain, flags, weights, layer, n_dev):
    dates, tokens, width = tokens_in.shape
    per_head = n_dev // HEADS
    rows = HEAD // per_head
    block = 4 * HEAD

    def body(x_ref, g_ref, m_ref, wk_ref, wv_ref, o_ref):
        t = pl.program_id(0)
        xf = x_ref[0].astype(jnp.float32)
        in_msq = jnp.mean(xf * xf, -1, keepdims=True) + 1e-05
        x = (xf * lax.rsqrt(in_msq) * g_ref[...]).astype(jnp.bfloat16)
        u = jnp.dot(x, wk_ref[0], preferred_element_type=jnp.float32)
        key = jnp.where(u > 0, u + 1.0, jnp.exp(jnp.minimum(u, 0.0))) * m_ref[0]
        key = key.astype(jnp.bfloat16)
        value = jnp.dot(x, wv_ref[0], preferred_element_type=jnp.float32).astype(jnp.bfloat16)
        blocks = [
            lax.dot_general(
                key[:, b * block : (b + 1) * block],
                value[:, b * block : (b + 1) * block],
                (((0,), (0,)), ((), ())),
                preferred_element_type=jnp.float32,
            )
            for b in range(width // block)
        ]
        for date in range(dates):

            @pl.when(t == date)
            def _():
                for b, kv in enumerate(blocks):
                    for i in range(block // HEAD):
                        h = b * (block // HEAD) + i
                        for rb in range(per_head):
                            o_ref[h * per_head + rb, :, date * HEAD : (date + 1) * HEAD] = kv[
                                i * HEAD + rb * rows : i * HEAD + (rb + 1) * rows,
                                i * HEAD : (i + 1) * HEAD,
                            ]

    return pl.pallas_call(
        body,
        grid=(dates,),
        out_shape=jax.ShapeDtypeStruct((n_dev, rows, dates * HEAD), jnp.float32),
        in_specs=[
            pl.BlockSpec((1, tokens, width), lambda t: (t, 0, 0)),
            pl.BlockSpec((1, width), lambda t: (0, 0)),
            pl.BlockSpec((1, tokens, 1), lambda t: (t, 0, 0)),
            pl.BlockSpec((1, width, width), lambda t: (layer, 0, 1)),
            pl.BlockSpec((1, width, width), lambda t: (layer, 0, 2)),
        ],
        out_specs=pl.BlockSpec((n_dev, rows, dates * HEAD), lambda t: (0, 0, 0)),
        compiler_params=pltpu.CompilerParams(dimension_semantics=("arbitrary",)),
    )(tokens_in, gain, flags, weights, weights)


def shards(frames, cloud_mask, qkv_weight, out_weight, norm_gain, head_norm_scale, decay):
    dates_here, tokens_here, width = frames.shape
    heads = HEADS
    n_space = lax.axis_size("space")
    n_date = lax.axis_size("date")
    n_dev = n_date * n_space
    everyone = ("date", "space")
    me = lax.axis_index("date") * n_space + lax.axis_index("space")
    entries = heads * HEAD * HEAD // n_dev
    per_head = n_dev // heads
    dates_all = n_date * dates_here
    to_each = jnp.repeat(jnp.transpose(decay, (2, 0, 1)), per_head, axis=0)
    from_each = lax.all_to_all(to_each, everyone, 0, 0, tiled=True)
    my_decay = from_each.reshape(n_date, n_space, STACK_LEVELS, dates_here)[:, 0]
    my_decay = jnp.transpose(my_decay, (1, 0, 2)).reshape(STACK_LEVELS, dates_all)
    pos = jnp.arange(dates_all)
    current = frames
    flag_f = cloud_mask.astype(jnp.float32)[:, :, None]
    for layer in range(STACK_LEVELS):
        xf = current.astype(jnp.float32)
        in_msq = jnp.mean(xf * xf, -1, keepdims=True) + 1e-05
        normalized_output = (xf * lax.rsqrt(in_msq) * norm_gain[layer]).astype(jnp.bfloat16)
        flat = normalized_output.reshape(-1, width)
        pieces = lax.all_to_all(
            kv_chunks(current, norm_gain[layer][None, :], flag_f, qkv_weight, layer, n_dev), everyone, 0, 0, tiled=True
        )
        rows = pieces.shape[1]
        kv = pieces.reshape(n_date, n_space, rows, dates_here * HEAD).sum(1)
        kv = lax.optimization_barrier(kv).reshape(n_date, rows, dates_here, HEAD)
        kv = jnp.transpose(kv, (0, 2, 1, 3)).reshape(dates_all, entries)
        d = my_decay[layer]
        inside = (pos[None, None, :] > pos[None, :, None]) & (pos[None, None, :] <= pos[:, None, None])
        weight = jnp.prod(jnp.where(inside, d[None, None, :], 1.0), axis=2)
        weight = jnp.where(pos[None, :] <= pos[:, None], weight, 0.0)
        states = jnp.dot(weight, kv, precision=lax.Precision.HIGHEST, preferred_element_type=jnp.float32)
        proj_q = jnp.dot(flat, qkv_weight[layer, :, :width], preferred_element_type=jnp.float32)
        query = (
            feature(proj_q)
            .astype(jnp.bfloat16)
            .reshape(dates_here, tokens_here, heads, HEAD)
        )
        states, query = lax.optimization_barrier((states, query))
        state_b = states.astype(jnp.bfloat16).reshape(n_date, 1, dates_here, entries)
        outgoing = jnp.broadcast_to(state_b, (n_date, n_space, dates_here, entries)).reshape(
            n_dev, dates_here, entries
        )
        back = lax.all_to_all(outgoing, everyone, 0, 0, tiled=True)
        state_b = jnp.transpose(back, (1, 0, 2)).reshape(dates_here, heads, HEAD, HEAD)

        numer = jnp.einsum("tshe,thef->tshf", query, state_b, preferred_element_type=jnp.float32)
        head_msq = jnp.mean(numer * numer, -1, keepdims=True) + 1e-05
        numer = numer * lax.rsqrt(head_msq)
        mixed = (numer.reshape(dates_here, tokens_here, width) * head_norm_scale[layer]).astype(
            jnp.bfloat16
        )
        update = jnp.dot(
            mixed.reshape(-1, width), out_weight[layer], preferred_element_type=jnp.float32
        )
        current = (xf + update.reshape(dates_here, tokens_here, width)).astype(jnp.bfloat16)
    return current


def solution(mesh):
    placed = (
        P("date", "space", None),
        P("date", "space"),
        P(),
        P(),
        P(),
        P(),
        P(None, "date", None),
    )
    return jax.shard_map(
        shards, mesh=mesh, in_specs=placed, out_specs=P("date", "space", None), check_vma=False
    )
```

```python
import jax
import jax.numpy as jnp
from jax import lax
from jax.experimental import pallas as pl
from jax.experimental.pallas import tpu as pltpu
from jax.sharding import PartitionSpec as P

HEADS = 16
HEAD = 64
STACK_LEVELS = 2


def feature(u):
    return jax.nn.elu(u) + 1.0


def kv_chunks(tokens_in, gain, flags, weights, layer, n_dev):
    dates, tokens, width = tokens_in.shape
    per_head = n_dev // HEADS
    rows = HEAD // per_head
    block = 4 * HEAD

    def body(x_ref, g_ref, m_ref, wk_ref, wv_ref, o_ref):
        t = pl.program_id(0)
        xf = x_ref[0].astype(jnp.float32)
        in_msq = jnp.mean(xf * xf, -1, keepdims=True) + 1e-05
        x = (xf * lax.rsqrt(in_msq) * g_ref[...]).astype(jnp.bfloat16)
        u = jnp.dot(x, wk_ref[0], preferred_element_type=jnp.float32)
        key = jnp.where(u > 0, u + 1.0, jnp.exp(jnp.minimum(u, 0.0))) * m_ref[0]
        key = key.astype(jnp.bfloat16)
        value = jnp.dot(x, wv_ref[0], preferred_element_type=jnp.float32).astype(jnp.bfloat16)
        blocks = [
            lax.dot_general(
                key[:, b * block : (b + 1) * block],
                value[:, b * block : (b + 1) * block],
                (((0,), (0,)), ((), ())),
                preferred_element_type=jnp.float32,
            )
            for b in range(width // block)
        ]
        for date in range(dates):

            @pl.when(t == date)
            def _():
                for b, kv in enumerate(blocks):
                    for i in range(block // HEAD):
                        h = b * (block // HEAD) + i
                        for rb in range(per_head):
                            o_ref[h * per_head + rb, :, date * HEAD : (date + 1) * HEAD] = kv[
                                i * HEAD + rb * rows : i * HEAD + (rb + 1) * rows,
                                i * HEAD : (i + 1) * HEAD,
                            ]

    return pl.pallas_call(
        body,
        grid=(dates,),
        out_shape=jax.ShapeDtypeStruct((n_dev, rows, dates * HEAD), jnp.float32),
        in_specs=[
            pl.BlockSpec((1, tokens, width), lambda t: (t, 0, 0)),
            pl.BlockSpec((1, width), lambda t: (0, 0)),
            pl.BlockSpec((1, tokens, 1), lambda t: (t, 0, 0)),
            pl.BlockSpec((1, width, width), lambda t: (layer, 0, 1)),
            pl.BlockSpec((1, width, width), lambda t: (layer, 0, 2)),
        ],
        out_specs=pl.BlockSpec((n_dev, rows, dates * HEAD), lambda t: (0, 0, 0)),
        compiler_params=pltpu.CompilerParams(dimension_semantics=("arbitrary",)),
    )(tokens_in, gain, flags, weights, weights)


def shards(frames, cloud_mask, qkv_weight, out_weight, norm_gain, head_norm_scale, decay):
    dates_here, tokens_here, width = frames.shape
    heads = HEADS
    n_space = lax.axis_size("space")
    n_date = lax.axis_size("date")
    n_dev = n_date * n_space
    everyone = ("date", "space")
    me = lax.axis_index("date") * n_space + lax.axis_index("space")
    entries = heads * HEAD * HEAD // n_dev
    per_head = n_dev // heads
    dates_all = n_date * dates_here
    to_each = jnp.repeat(jnp.transpose(decay, (2, 0, 1)), per_head, axis=0)
    from_each = lax.all_to_all(to_each, everyone, 0, 0, tiled=True)
    my_decay = from_each.reshape(n_date, n_space, STACK_LEVELS, dates_here)[:, 0]
    my_decay = jnp.transpose(my_decay, (1, 0, 2)).reshape(STACK_LEVELS, dates_all)
    pos = jnp.arange(dates_all)
    current = frames
    flag_f = cloud_mask.astype(jnp.float32)[:, :, None]
    for layer in range(STACK_LEVELS):
        chunks = kv_chunks(current, norm_gain[layer][None, :], flag_f, qkv_weight, layer, n_dev)
        pieces = lax.all_to_all(chunks, everyone, 0, 0, tiled=True)
        chunks, current = lax.optimization_barrier((chunks, current))
        xf = current.astype(jnp.float32)
        in_msq = jnp.mean(xf * xf, -1, keepdims=True) + 1e-05
        normalized_output = (xf * lax.rsqrt(in_msq) * norm_gain[layer]).astype(jnp.bfloat16)
        flat = normalized_output.reshape(-1, width)
        rows = pieces.shape[1]
        kv = pieces.reshape(n_date, n_space, rows, dates_here * HEAD).sum(1)
        kv = lax.optimization_barrier(kv).reshape(n_date, rows, dates_here, HEAD)
        kv = jnp.transpose(kv, (0, 2, 1, 3)).reshape(dates_all, entries)
        d = my_decay[layer]
        inside = (pos[None, None, :] > pos[None, :, None]) & (pos[None, None, :] <= pos[:, None, None])
        weight = jnp.prod(jnp.where(inside, d[None, None, :], 1.0), axis=2)
        weight = jnp.where(pos[None, :] <= pos[:, None], weight, 0.0)
        states = jnp.dot(weight, kv, precision=lax.Precision.HIGHEST, preferred_element_type=jnp.float32)
        proj_q = jnp.dot(flat, qkv_weight[layer, :, :width], preferred_element_type=jnp.float32)
        query = (
            feature(proj_q)
            .astype(jnp.bfloat16)
            .reshape(dates_here, tokens_here, heads, HEAD)
        )
        states, query = lax.optimization_barrier((states, query))
        state_b = states.astype(jnp.bfloat16).reshape(n_date, 1, dates_here, entries)
        outgoing = jnp.broadcast_to(state_b, (n_date, n_space, dates_here, entries)).reshape(
            n_dev, dates_here, entries
        )
        back = lax.all_to_all(outgoing, everyone, 0, 0, tiled=True)
        state_b = jnp.transpose(back, (1, 0, 2)).reshape(dates_here, heads, HEAD, HEAD)

        numer = jnp.einsum("tshe,thef->tshf", query, state_b, preferred_element_type=jnp.float32)
        head_msq = jnp.mean(numer * numer, -1, keepdims=True) + 1e-05
        numer = numer * lax.rsqrt(head_msq)
        mixed = (numer.reshape(dates_here, tokens_here, width) * head_norm_scale[layer]).astype(
            jnp.bfloat16
        )
        update = jnp.dot(
            mixed.reshape(-1, width), out_weight[layer], preferred_element_type=jnp.float32
        )
        current = (xf + update.reshape(dates_here, tokens_here, width)).astype(jnp.bfloat16)
    return current


def solution(mesh):
    placed = (
        P("date", "space", None),
        P("date", "space"),
        P(),
        P(),
        P(),
        P(),
        P(None, "date", None),
    )
    return jax.shard_map(
        shards, mesh=mesh, in_specs=placed, out_specs=P("date", "space", None), check_vma=False
    )
```
